256 devices in a mesh: dp: 4 (over y), tp: 64 (over x, z, core).
Axes of the slice: x: 4, y: 4, z: 8, core: 2. Of those that a mesh axis runs over, the one named last changes fastest.
Arguments:
- attn_heads: bfloat16 [4, 8192, 2048], P(None, 'tp', 'dp'), may hold values from -1.5 to 1.5
- w_out: bfloat16 [2048, 2048], P('dp'), may hold values from -0.125 to 0.125
- residual: bfloat16 [32768, 2048], P(('dp', 'tp')), may hold values from -1.5 to 1.5
- moe_gain: float32 [2048], replicated, may hold values from 0.1 to 1.9
- router: bfloat16 [2048, 64], replicated, may hold values from -0.0625 to 0.0625
- expert_ids: int32 [32768, 8], P(('dp', 'tp')), may hold values from 0 to 63, all different within a row; in each aligned block of 128 rows (0 to 127, 128 to 255, ...) at most 24 rows name the same one
- w_gate_up: bfloat16 [64, 2048, 1024], P('tp'), may hold values from -0.125 to 0.125
- w_down: bfloat16 [64, 512, 2048], P('tp'), may hold values from -0.75 to 0.75
- next_gain: float32 [2048], replicated, may hold values from 0.1 to 1.9
Outputs:
- layer_out: bfloat16 [32768, 2048], P(('dp', 'tp'))
- next_input: bfloat16 [4, 8192, 2048], P(None, 'tp')
The draws below stay inside these ranges and needn't reach their ends.
Inputs may be any that keep to these rules, and one draw needn't show every extreme that they name: `expert_ids`: each row names 8 different experts. In each aligned block of 128 rows (the rows of one device) no expert is named by more than 24 rows, a bound that some block reaches.
All inputs are finite; a program needn't handle non-finite values.
Results may differ from the reference program's by a relative error of at most 0.0095.
Values may be sent and summed in bfloat16 or wider, within the bound.
No kernel may reach another device: no remote copies, remote signals or barrier semaphores. Data moves between devices by JAX's collectives and lax.ppermute only.
A program may use at most 128 MiB of HBM per device.

```python
import math
import jax
import jax.numpy as jnp
import numpy as np
from jax import lax

D = 2048
TOP = 8
H = 512
TOK_DEV = 128
EXPERTS = 64
MOST = 24
SEG = 8192
TOKENS = 32768
N_DP = 4


def steps_of(rng, extent, split, smallest, top_value):
    level = 1.0
    for position, parts in split:
        draws = jax.random.uniform(jax.random.fold_in(jax.random.fold_in(rng, 6), position), (parts,), jnp.float32, smallest / len(split), top_value / len(split))
        level = level * jnp.repeat(jnp.exp(draws), extent[position] // parts).reshape((-1,) + (1,) * (len(extent) - 1 - position))
    return level


def assign_block(stream_key, own, number, rows, number_of, top, reach, lean):
    sequence = jax.random.permutation(stream_key, number_of)
    packed, ordinary = shares(number_of, rows * top, reach, lean, True), shares(number_of, rows * top, reach, lean, False)
    places = jnp.arange(number_of)

    def named(lengths, turn):
        used = int((lengths > 0).sum())
        fixed = max(1, used // 4)
        shifted = fixed + (places - fixed + turn * (used - fixed)) % max(1, number_of - fixed)
        return jnp.zeros((number_of,), jnp.int32).at[sequence[jnp.where(places < fixed, places, shifted)]].set(jnp.asarray(lengths, jnp.int32))

    lengths = jnp.where(number % 4 == 0, named(packed, number // 4), named(ordinary, number - number // 4 - 1))
    mixed = jax.random.permutation(jax.random.fold_in(own, 3), number_of)
    source_of, sink = mixed[0:number_of // 2 * 2:2], mixed[1:number_of // 2 * 2:2]
    room = jnp.minimum(lengths[source_of] - 1, reach - lengths[sink]) // 2
    room = jnp.where((source_of == sequence[0]) | (sink == sequence[0]) | (lengths[sink] == 0), 0, jnp.maximum(room, 0))
    shifted = jax.random.randint(jax.random.fold_in(own, 4), (number_of // 2,), 0, 1 << 20) % (room + 1)
    lengths = lengths.at[source_of].add(-shifted).at[sink].add(shifted)
    members = jnp.searchsorted(jnp.cumsum(lengths), jnp.arange(rows * top), side="right").astype(jnp.int32)
    listing = members.reshape(top, rows).T
    listing = listing[jax.random.permutation(jax.random.fold_in(own, 1), rows)]
    turn = jax.random.randint(jax.random.fold_in(own, 2), (rows, 1), 0, top)
    return jnp.take_along_axis(listing, (jnp.arange(top)[None, :] + turn) % top, axis=1)


def shares(count, total, limit, lean, full):
    loads = [(1 << 20) // math.isqrt(rank ** lean) + 1 for rank in range(1, count + 1)]
    largest = limit if full else min(limit, max(-(-total // count), total * loads[0] // sum(loads)))
    least = 1 if total - largest >= count - 1 else 0
    holding, surplus = [largest] + [least] * (count - 1), total - largest - least * (count - 1)
    while surplus > 0:
        movable = [i for i in range(1, count) if holding[i] < largest] or [i for i in range(1, count) if holding[i] < limit]
        whole, budget = sum([loads[i] for i in movable]), surplus
        for i in movable:
            addition = min(limit - holding[i], max(1, budget * loads[i] // whole), surplus)
            holding[i] = holding[i] + addition
            surplus = surplus - addition
    return np.array(holding)


def scatter_about(rng, dims, spread, limit, shards=(), kind=jnp.bfloat16):
    entries = jax.random.normal(rng, dims, jnp.float32) * spread
    if len(shards) > 0:
        entries = steps_of(rng, dims, shards, -0.22, 0.18) * entries
    return jnp.clip(entries, min=-limit, max=limit).astype(kind)


def setup_inputs(seed: int = 0) -> dict:
    key_of = jax.random.split(jax.random.key(seed), 10)
    attn_heads = scatter_about(key_of[0], (N_DP, SEG, D), 0.25, 1.5, ((1, 64), (2, 4)))
    w_out = scatter_about(key_of[1], (D, D), D ** -0.5, 0.125, ((0, 4),))
    residual = scatter_about(key_of[2], (TOKENS, D), 0.25, 1.5, ((0, 256),))
    moe_gain = jnp.clip(1.0 + 0.18 * jax.random.normal(key_of[3], (D,), jnp.float32), 0.1, 1.9)
    router = scatter_about(key_of[4], (D, EXPERTS), (4 * D) ** -0.5, 0.0625)
    expert_ids_keys = jax.random.split(jax.random.fold_in(key_of[5], 1), TOKENS // TOK_DEV)
    expert_ids_turns = jax.random.permutation(jax.random.fold_in(key_of[5], 3), TOKENS // TOK_DEV)
    expert_ids = jax.vmap(lambda own, number: assign_block(jax.random.fold_in(key_of[5], 2), own, number, TOK_DEV, EXPERTS, TOP, MOST, 4))(expert_ids_keys, expert_ids_turns).reshape((TOKENS, TOP))
    w_gate_up = scatter_about(key_of[6], (EXPERTS, D, 2 * H), D ** -0.5, 0.125, ((0, 64),))
    w_down = scatter_about(key_of[7], (EXPERTS, H, D), (H // 8) ** -0.5, 0.75, ((0, 64),))
    next_gain = jnp.clip(1.0 + 0.18 * jax.random.normal(key_of[8], (D,), jnp.float32), 0.1, 1.9)
    return dict(attn_heads=attn_heads, w_out=w_out, residual=residual, moe_gain=moe_gain, router=router, expert_ids=expert_ids, w_gate_up=w_gate_up, w_down=w_down, next_gain=next_gain)


EPS = 1e-05

def rms_scale(values, gain_vector):
    mean_square = lax.optimization_barrier(jnp.mean(values * values, axis=-1, keepdims=True))
    return values * lax.rsqrt(mean_square + EPS) * gain_vector

def expert_block(row_block, gate_up, down_proj):
    hidden_width = down_proj.shape[0]
    projected_up = jnp.dot(row_block, gate_up, preferred_element_type=jnp.float32)
    activated = (jax.nn.silu(projected_up[:, :hidden_width]) * projected_up[:, hidden_width:]).astype(jnp.bfloat16)
    return jnp.dot(activated, down_proj, preferred_element_type=jnp.float32).astype(jnp.bfloat16)

def reference(attn_heads, w_out, residual, moe_gain, router, expert_ids, w_gate_up, w_down, next_gain):
    flat_heads = attn_heads.reshape(TOKENS, D)
    projected = jnp.dot(flat_heads, w_out, preferred_element_type=jnp.float32)
    mid_state = (residual.astype(jnp.float32) + projected).astype(jnp.bfloat16)
    mid_wide = mid_state.astype(jnp.float32)
    normed = rms_scale(mid_wide, moe_gain).astype(jnp.bfloat16)
    logits = jnp.dot(normed, router, preferred_element_type=jnp.float32)
    picked = jnp.take_along_axis(logits, expert_ids, axis=1)
    raised = jnp.exp(picked)
    gate_weights = raised / lax.optimization_barrier(jnp.sum(raised, axis=1, keepdims=True))
    expert_pos = jnp.arange(EXPERTS, dtype=jnp.int32)
    member = jnp.zeros((TOKENS, EXPERTS), jnp.int32)
    weight_full = jnp.zeros((TOKENS, EXPERTS), jnp.float32)
    for slot_choice in range(TOP):
        match_now = expert_ids[:, slot_choice:slot_choice + 1] == expert_pos[None, :]
        member = member + match_now.astype(jnp.int32)
        weight_full = weight_full + jnp.where(match_now, gate_weights[:, slot_choice:slot_choice + 1], 0.0)
    blocks = TOKENS // TOK_DEV
    member_blocks = member.reshape(blocks, TOK_DEV, EXPERTS)
    row_ranks = jnp.cumsum(member_blocks, axis=1, dtype=jnp.int32) - member_blocks
    row_pos = jnp.arange(TOK_DEV, dtype=jnp.int32)
    slot_pos = jnp.arange(MOST, dtype=jnp.int32)
    block_base = jnp.arange(blocks, dtype=jnp.int32) * TOK_DEV

    def one_expert(expert_sum, pieces):
        gate_up, down_proj, member_col, rank_col, weight_col = pieces
        placed = (member_col[:, None, :] > 0) & (rank_col[:, None, :] == slot_pos[None, :, None])
        local_row = lax.optimization_barrier(jnp.sum(jnp.where(placed, row_pos[None, None, :], 0), axis=2, dtype=jnp.int32))
        filled = jnp.any(placed, axis=2).reshape(-1)
        row_index = (block_base[:, None] + local_row).reshape(-1).astype(jnp.int32)
        inputs = jnp.take(normed, row_index, axis=0)
        outputs = expert_block(inputs, gate_up, down_proj)
        row_scale = jnp.where(filled, jnp.take(weight_col, row_index), 0.0)
        expert_sum = expert_sum.at[row_index].add(row_scale[:, None] * outputs.astype(jnp.float32))
        return (expert_sum, None)
    pieces = (w_gate_up, w_down, jnp.transpose(member_blocks, (2, 0, 1)), jnp.transpose(row_ranks, (2, 0, 1)), weight_full.T)
    expert_sum, unused = lax.scan(one_expert, jnp.zeros((TOKENS, D), jnp.float32), pieces)
    layer_sum = mid_wide + expert_sum
    layer_out = layer_sum.astype(jnp.bfloat16)
    next_input = rms_scale(layer_sum, next_gain).astype(jnp.bfloat16).reshape(N_DP, SEG, D)
    return (layer_out, next_input)
```

```python
import jax
import jax.numpy as jnp
from jax import lax
from jax.sharding import PartitionSpec as P

EPS = 1e-05
CHUNKS = 4


def rms_scale(values, gain_vector):
    mean_square = jnp.mean(values * values, axis=-1, keepdims=True)
    return values * lax.rsqrt(mean_square + EPS) * gain_vector


def split_hi_lo(values):
    high = values.astype(jnp.bfloat16)
    low = (values - high.astype(jnp.float32)).astype(jnp.bfloat16)
    return high, low


def local(attn_heads, w_out, residual, moe_gain, router, expert_ids, w_gate_up, w_down, next_gain):
    groups, tok_rows, quarter = attn_heads.shape
    feat_width = w_out.shape[1]
    experts = router.shape[1]
    top_count = expert_ids.shape[1]
    capacity = min(tok_rows, 3 * tok_rows * top_count // (2 * experts))
    slots = experts * capacity
    step = feat_width // CHUNKS

    expert_pos = jnp.arange(experts, dtype=jnp.int32)
    chosen = expert_ids[:, :, None] == expert_pos[None, None, :]
    member = jnp.sum(chosen.astype(jnp.float32), axis=1)
    row_pos = jnp.arange(tok_rows, dtype=jnp.int32)
    earlier = (row_pos[None, :] < row_pos[:, None]).astype(jnp.bfloat16)
    row_ranks = jnp.dot(
        earlier, member.astype(jnp.bfloat16), preferred_element_type=jnp.float32
    ).astype(jnp.int32)
    slot_pos = jnp.arange(capacity, dtype=jnp.int32)
    placed = (member.T[:, None, :] > 0) & (row_ranks.T[:, None, :] == slot_pos[None, :, None])
    dispatch = placed.reshape(slots, tok_rows).astype(jnp.bfloat16)

    flat_heads = attn_heads.reshape(groups * tok_rows, quarter)
    partials = [
        jnp.dot(flat_heads, w_out[:, c * step : (c + 1) * step], preferred_element_type=jnp.float32)
        for c in range(CHUNKS)
    ]
    part = lax.psum_scatter(partials[0], "dp", scatter_dimension=0, tiled=True)
    mid_parts = []
    arrived_parts = []
    for c in range(CHUNKS):
        cols = slice(c * step, (c + 1) * step)
        res_c, part = lax.optimization_barrier((residual[:, cols], part))
        mid_c = (res_c.astype(jnp.float32) + part).astype(jnp.bfloat16)
        mid_parts.append(mid_c)
        outgoing = jnp.dot(dispatch, mid_c, preferred_element_type=jnp.float32).astype(jnp.bfloat16)
        if c + 1 < CHUNKS:
            outgoing, following = lax.optimization_barrier((outgoing, partials[c + 1]))
            part = lax.psum_scatter(following, "dp", scatter_dimension=0, tiled=True)
        arrived_parts.append(
            lax.all_to_all(
                outgoing.reshape(experts, capacity, step), "tp", split_axis=0, concat_axis=0, tiled=True
            ).reshape(slots, step)
        )

    mid_state = jnp.concatenate(mid_parts, axis=1)
    mid_wide = mid_state.astype(jnp.float32)
    normed = rms_scale(mid_wide, moe_gain).astype(jnp.bfloat16)
    logits = jnp.dot(normed, router, preferred_element_type=jnp.float32)
    picked = jnp.sum(jnp.where(chosen, logits[:, None, :], 0.0), axis=2)
    raised = jnp.exp(picked)
    gate_weights = raised / jnp.sum(raised, axis=1, keepdims=True)
    weight_full = jnp.sum(jnp.where(chosen, gate_weights[:, :, None], 0.0), axis=1)
    combine = jnp.where(placed, weight_full.T[:, None, :], 0.0).reshape(slots, tok_rows)
    combine_hi, combine_lo = split_hi_lo(combine)

    arrived = jnp.concatenate(arrived_parts, axis=1).astype(jnp.float32)
    arrived_normed = rms_scale(arrived, moe_gain).astype(jnp.bfloat16)
    gate_up = w_gate_up[0]
    down_proj = w_down[0]
    hidden_width = down_proj.shape[0]
    projected_up = jnp.dot(arrived_normed, gate_up, preferred_element_type=jnp.float32)
    activated = (
        jax.nn.silu(projected_up[:, :hidden_width]) * projected_up[:, hidden_width:]
    ).astype(jnp.bfloat16)

    sum_parts = []
    for c in range(CHUNKS):
        cols = slice(c * step, (c + 1) * step)
        served = jnp.dot(activated, down_proj[:, cols], preferred_element_type=jnp.float32).astype(
            jnp.bfloat16
        )
        returned = lax.all_to_all(
            served.reshape(experts, capacity, step), "tp", split_axis=0, concat_axis=0, tiled=True
        ).reshape(slots, step)
        dims = (((0,), (0,)), ((), ()))
        expert_sum = lax.dot_general(
            combine_hi, returned, dims, preferred_element_type=jnp.float32
        ) + lax.dot_general(combine_lo, returned, dims, preferred_element_type=jnp.float32)
        sum_parts.append(mid_wide[:, cols] + expert_sum)

    layer_sum = jnp.concatenate(sum_parts, axis=1)
    layer_out = layer_sum.astype(jnp.bfloat16)
    next_local = rms_scale(layer_sum, next_gain).astype(jnp.bfloat16)
    next_input = lax.all_gather(next_local[None], "dp", axis=0, tiled=True)
    return (layer_out, next_input)


def solution(mesh):
    in_specs = (
        P(None, "tp", "dp"),
        P("dp", None),
        P(("dp", "tp"), None),
        P(),
        P(),
        P(("dp", "tp"), None),
        P("tp", None, None),
        P("tp", None, None),
        P(),
    )
    out_specs = (P(("dp", "tp"), None), P(None, "tp", None))
    return jax.shard_map(local, mesh=mesh, in_specs=in_specs, out_specs=out_specs, check_vma=False)
```

```python
import jax
import jax.numpy as jnp
from jax import lax
from jax.sharding import PartitionSpec as P

EPS = 1e-05


def rms_scale(values, gain_vector):
    mean_square = jnp.mean(values * values, axis=-1, keepdims=True)
    return values * lax.rsqrt(mean_square + EPS) * gain_vector


def split_hi_lo(values):
    high = values.astype(jnp.bfloat16)
    low = (values - high.astype(jnp.float32)).astype(jnp.bfloat16)
    return high, low


def local(attn_heads, w_out, residual, moe_gain, router, expert_ids, w_gate_up, w_down, next_gain):
    groups, tok_rows, quarter = attn_heads.shape
    feat_width = w_out.shape[1]
    experts = router.shape[1]
    top_count = expert_ids.shape[1]
    capacity = min(tok_rows, 3 * tok_rows * top_count // (2 * experts))
    slots = experts * capacity

    flat_heads = attn_heads.reshape(groups * tok_rows, quarter)
    partial = jnp.dot(flat_heads, w_out, preferred_element_type=jnp.float32)
    pieces = lax.all_to_all(
        partial.reshape(groups, tok_rows, feat_width), "dp", split_axis=0, concat_axis=0, tiled=True
    )
    projected = jnp.sum(pieces, axis=0)
    mid_wide = (residual.astype(jnp.float32) + projected).astype(jnp.bfloat16).astype(jnp.float32)
    normed = rms_scale(mid_wide, moe_gain).astype(jnp.bfloat16)
    logits = jnp.dot(normed, router, preferred_element_type=jnp.float32)

    expert_pos = jnp.arange(experts, dtype=jnp.int32)
    chosen = expert_ids[:, :, None] == expert_pos[None, None, :]
    member = jnp.sum(chosen.astype(jnp.float32), axis=1)
    row_pos = jnp.arange(tok_rows, dtype=jnp.int32)
    earlier = (row_pos[None, :] < row_pos[:, None]).astype(jnp.bfloat16)
    row_ranks = jnp.dot(
        earlier, member.astype(jnp.bfloat16), preferred_element_type=jnp.float32
    ).astype(jnp.int32)
    slot_pos = jnp.arange(capacity, dtype=jnp.int32)
    placed = (member.T[:, None, :] > 0) & (row_ranks.T[:, None, :] == slot_pos[None, :, None])
    dispatch = placed.reshape(slots, tok_rows).astype(jnp.bfloat16)

    picked = jnp.sum(jnp.where(chosen, logits[:, None, :], 0.0), axis=2)
    raised = jnp.exp(picked)
    gate_weights = raised / jnp.sum(raised, axis=1, keepdims=True)
    weight_full = jnp.sum(jnp.where(chosen, gate_weights[:, :, None], 0.0), axis=1)
    combine = jnp.where(placed, weight_full.T[:, None, :], 0.0).reshape(slots, tok_rows)
    combine_hi, combine_lo = split_hi_lo(combine)

    outgoing = jnp.dot(dispatch, normed, preferred_element_type=jnp.float32).astype(jnp.bfloat16)
    arrived = lax.all_to_all(
        outgoing.reshape(experts, capacity, feat_width), "tp", split_axis=0, concat_axis=0, tiled=True
    ).reshape(slots, feat_width)

    gate_up = w_gate_up[0]
    down_proj = w_down[0]
    hidden_width = down_proj.shape[0]
    projected_up = jnp.dot(arrived, gate_up, preferred_element_type=jnp.float32)
    activated = (
        jax.nn.silu(projected_up[:, :hidden_width]) * projected_up[:, hidden_width:]
    ).astype(jnp.bfloat16)
    served = jnp.dot(activated, down_proj, preferred_element_type=jnp.float32).astype(jnp.bfloat16)

    returned = lax.all_to_all(
        served.reshape(experts, capacity, feat_width), "tp", split_axis=0, concat_axis=0, tiled=True
    ).reshape(slots, feat_width)
    dims = (((0,), (0,)), ((), ()))
    expert_sum = lax.dot_general(
        combine_hi, returned, dims, preferred_element_type=jnp.float32
    ) + lax.dot_general(combine_lo, returned, dims, preferred_element_type=jnp.float32)

    layer_sum = mid_wide + expert_sum
    layer_out = layer_sum.astype(jnp.bfloat16)
    next_local = rms_scale(layer_sum, next_gain).astype(jnp.bfloat16)
    copies = jnp.broadcast_to(next_local[None], (groups, tok_rows, feat_width))
    next_input = lax.all_to_all(copies, "dp", split_axis=0, concat_axis=0, tiled=True)
    return (layer_out, next_input)


def solution(mesh):
    in_specs = (
        P(None, "tp", "dp"),
        P("dp", None),
        P(("dp", "tp"), None),
        P(),
        P(),
        P(("dp", "tp"), None),
        P("tp", None, None),
        P("tp", None, None),
        P(),
    )
    out_specs = (P(("dp", "tp"), None), P(None, "tp", None))
    return jax.shard_map(local, mesh=mesh, in_specs=in_specs, out_specs=out_specs, check_vma=False)
```

```python
import jax
import jax.numpy as jnp
from jax import lax
from jax.sharding import PartitionSpec as P

EPS = 1e-05


def rms_scale(values, gain_vector):
    mean_square = jnp.mean(values * values, axis=-1, keepdims=True)
    return values * lax.rsqrt(mean_square + EPS) * gain_vector


def split_hi_lo(values):
    high = values.astype(jnp.bfloat16)
    low = (values - high.astype(jnp.float32)).astype(jnp.bfloat16)
    return high, low


def local(attn_heads, w_out, residual, moe_gain, router, expert_ids, w_gate_up, w_down, next_gain):
    groups, tok_rows, quarter = attn_heads.shape
    feat_width = w_out.shape[1]
    experts = router.shape[1]
    top_count = expert_ids.shape[1]
    capacity = min(tok_rows, 3 * tok_rows * top_count // (2 * experts))
    slots = experts * capacity

    expert_pos = jnp.arange(experts, dtype=jnp.int32)
    chosen = expert_ids[:, :, None] == expert_pos[None, None, :]
    member = jnp.sum(chosen.astype(jnp.float32), axis=1)
    row_pos = jnp.arange(tok_rows, dtype=jnp.int32)
    earlier = (row_pos[None, :] < row_pos[:, None]).astype(jnp.bfloat16)
    row_ranks = jnp.dot(
        earlier, member.astype(jnp.bfloat16), preferred_element_type=jnp.float32
    ).astype(jnp.int32)
    slot_pos = jnp.arange(capacity, dtype=jnp.int32)
    placed = (member.T[:, None, :] > 0) & (row_ranks.T[:, None, :] == slot_pos[None, :, None])
    dispatch = placed.reshape(slots, tok_rows).astype(jnp.bfloat16)

    half = feat_width // 2
    flat_heads = attn_heads.reshape(groups * tok_rows, quarter)
    partials = [
        jnp.dot(flat_heads, w_out[:, c * half : (c + 1) * half], preferred_element_type=jnp.float32)
        for c in range(2)
    ]
    pieces = lax.all_to_all(
        partials[0].reshape(groups, tok_rows, half), "dp", split_axis=0, concat_axis=0, tiled=True
    )
    part = jnp.sum(pieces, axis=0)
    mid_parts = []
    arrived_parts = []
    for c in range(2):
        cols = slice(c * half, (c + 1) * half)
        res_c, part = lax.optimization_barrier((residual[:, cols], part))
        mid_c = (res_c.astype(jnp.float32) + part).astype(jnp.bfloat16)
        mid_parts.append(mid_c)
        outgoing = jnp.dot(dispatch, mid_c, preferred_element_type=jnp.float32).astype(jnp.bfloat16)
        if c == 0:
            outgoing, following = lax.optimization_barrier((outgoing, partials[1]))
            part = lax.psum_scatter(following, "dp", scatter_dimension=0, tiled=True)
        arrived_parts.append(
            lax.all_to_all(
                outgoing.reshape(experts, capacity, half), "tp", split_axis=0, concat_axis=0, tiled=True
            ).reshape(slots, half)
        )
    mid_wide = jnp.concatenate(mid_parts, axis=1).astype(jnp.float32)
    normed = rms_scale(mid_wide, moe_gain).astype(jnp.bfloat16)
    logits = jnp.dot(normed, router, preferred_element_type=jnp.float32)

    picked = jnp.sum(jnp.where(chosen, logits[:, None, :], 0.0), axis=2)
    raised = jnp.exp(picked)
    gate_weights = raised / jnp.sum(raised, axis=1, keepdims=True)
    weight_full = jnp.sum(jnp.where(chosen, gate_weights[:, :, None], 0.0), axis=1)
    combine = jnp.where(placed, weight_full.T[:, None, :], 0.0).reshape(slots, tok_rows)
    combine_hi, combine_lo = split_hi_lo(combine)

    arrived_mid = jnp.concatenate(arrived_parts, axis=1).astype(jnp.float32)
    arrived = rms_scale(arrived_mid, moe_gain).astype(jnp.bfloat16)

    gate_up = w_gate_up[0]
    down_proj = w_down[0]
    hidden_width = down_proj.shape[0]
    projected_up = jnp.dot(arrived, gate_up, preferred_element_type=jnp.float32)
    activated = (
        jax.nn.silu(projected_up[:, :hidden_width]) * projected_up[:, hidden_width:]
    ).astype(jnp.bfloat16)
    served = jnp.dot(activated, down_proj, preferred_element_type=jnp.float32).astype(jnp.bfloat16)

    returned = lax.all_to_all(
        served.reshape(experts, capacity, feat_width), "tp", split_axis=0, concat_axis=0, tiled=True
    ).reshape(slots, feat_width)
    dims = (((0,), (0,)), ((), ()))
    expert_sum = lax.dot_general(
        combine_hi, returned, dims, preferred_element_type=jnp.float32
    ) + lax.dot_general(combine_lo, returned, dims, preferred_element_type=jnp.float32)

    layer_sum = mid_wide + expert_sum
    layer_out = layer_sum.astype(jnp.bfloat16)
    next_local = rms_scale(layer_sum, next_gain).astype(jnp.bfloat16)
    copies = jnp.broadcast_to(next_local[None], (groups, tok_rows, feat_width))
    next_input = lax.all_to_all(copies, "dp", split_axis=0, concat_axis=0, tiled=True)
    return (layer_out, next_input)


def solution(mesh):
    in_specs = (
        P(None, "tp", "dp"),
        P("dp", None),
        P(("dp", "tp"), None),
        P(),
        P(),
        P(("dp", "tp"), None),
        P("tp", None, None),
        P("tp", None, None),
        P(),
    )
    out_specs = (P(("dp", "tp"), None), P(None, "tp", None))
    return jax.shard_map(local, mesh=mesh, in_specs=in_specs, out_specs=out_specs, check_vma=False)
```

```python
import jax
import jax.numpy as jnp
from jax import lax
from jax.sharding import PartitionSpec as P

EPS = 1e-05


def rms_scale(values, gain_vector):
    mean_square = jnp.mean(values * values, axis=-1, keepdims=True)
    return values * lax.rsqrt(mean_square + EPS) * gain_vector


def split_hi_lo(values):
    high = values.astype(jnp.bfloat16)
    low = (values - high.astype(jnp.float32)).astype(jnp.bfloat16)
    return high, low


def dp_reduce(blocks):
    ring = blocks.shape[0]
    here = lax.axis_index("dp")
    total = blocks[here]
    for shift in range(1, ring):
        sent = lax.dynamic_index_in_dim(blocks, (here + shift) % ring, axis=0, keepdims=False)
        pairs = [(j, (j + shift) % ring) for j in range(ring)]
        total = total + lax.ppermute(sent, "dp", pairs)
    return total


def local(attn_heads, w_out, residual, moe_gain, router, expert_ids, w_gate_up, w_down, next_gain):
    groups, tok_rows, quarter = attn_heads.shape
    feat_width = w_out.shape[1]
    experts = router.shape[1]
    top_count = expert_ids.shape[1]
    capacity = min(tok_rows, 3 * tok_rows * top_count // (2 * experts))
    slots = experts * capacity

    expert_pos = jnp.arange(experts, dtype=jnp.int32)
    chosen = expert_ids[:, :, None] == expert_pos[None, None, :]
    member = jnp.sum(chosen.astype(jnp.float32), axis=1)
    row_pos = jnp.arange(tok_rows, dtype=jnp.int32)
    earlier = (row_pos[None, :] < row_pos[:, None]).astype(jnp.bfloat16)
    row_ranks = jnp.dot(
        earlier, member.astype(jnp.bfloat16), preferred_element_type=jnp.float32
    ).astype(jnp.int32)
    slot_pos = jnp.arange(capacity, dtype=jnp.int32)
    placed = (member.T[:, None, :] > 0) & (row_ranks.T[:, None, :] == slot_pos[None, :, None])
    dispatch = placed.reshape(slots, tok_rows).astype(jnp.bfloat16)

    half = feat_width // 2
    flat_heads = attn_heads.reshape(groups * tok_rows, quarter)
    partials = [
        jnp.dot(flat_heads, w_out[:, c * half : (c + 1) * half], preferred_element_type=jnp.float32)
        for c in range(2)
    ]
    pieces = lax.all_to_all(
        partials[0].reshape(groups, tok_rows, half), "dp", split_axis=0, concat_axis=0, tiled=True
    )
    part = jnp.sum(pieces, axis=0)
    mid_parts = []
    arrived_parts = []
    for c in range(2):
        cols = slice(c * half, (c + 1) * half)
        res_c, part = lax.optimization_barrier((residual[:, cols], part))
        mid_c = (res_c.astype(jnp.float32) + part).astype(jnp.bfloat16)
        mid_parts.append(mid_c)
        outgoing = jnp.dot(dispatch, mid_c, preferred_element_type=jnp.float32).astype(jnp.bfloat16)
        if c == 0:
            outgoing, following = lax.optimization_barrier((outgoing, partials[1]))
            part = dp_reduce(following.reshape(groups, tok_rows, half))
        arrived_parts.append(
            lax.all_to_all(
                outgoing.reshape(experts, capacity, half), "tp", split_axis=0, concat_axis=0, tiled=True
            ).reshape(slots, half)
        )
    mid_wide = jnp.concatenate(mid_parts, axis=1).astype(jnp.float32)
    normed = rms_scale(mid_wide, moe_gain).astype(jnp.bfloat16)
    logits = jnp.dot(normed, router, preferred_element_type=jnp.float32)

    picked = jnp.sum(jnp.where(chosen, logits[:, None, :], 0.0), axis=2)
    raised = jnp.exp(picked)
    gate_weights = raised / jnp.sum(raised, axis=1, keepdims=True)
    weight_full = jnp.sum(jnp.where(chosen, gate_weights[:, :, None], 0.0), axis=1)
    combine = jnp.where(placed, weight_full.T[:, None, :], 0.0).reshape(slots, tok_rows)
    combine_hi, combine_lo = split_hi_lo(combine)

    arrived_mid = jnp.concatenate(arrived_parts, axis=1).astype(jnp.float32)
    arrived = rms_scale(arrived_mid, moe_gain).astype(jnp.bfloat16)

    gate_up = w_gate_up[0]
    down_proj = w_down[0]
    hidden_width = down_proj.shape[0]
    projected_up = jnp.dot(arrived, gate_up, preferred_element_type=jnp.float32)
    activated = (
        jax.nn.silu(projected_up[:, :hidden_width]) * projected_up[:, hidden_width:]
    ).astype(jnp.bfloat16)
    served = jnp.dot(activated, down_proj, preferred_element_type=jnp.float32).astype(jnp.bfloat16)

    returned = lax.all_to_all(
        served.reshape(experts, capacity, feat_width), "tp", split_axis=0, concat_axis=0, tiled=True
    ).reshape(slots, feat_width)
    dims = (((0,), (0,)), ((), ()))
    expert_sum = lax.dot_general(
        combine_hi, returned, dims, preferred_element_type=jnp.float32
    ) + lax.dot_general(combine_lo, returned, dims, preferred_element_type=jnp.float32)

    layer_sum = mid_wide + expert_sum
    layer_out = layer_sum.astype(jnp.bfloat16)
    next_local = rms_scale(layer_sum, next_gain).astype(jnp.bfloat16)
    copies = jnp.broadcast_to(next_local[None], (groups, tok_rows, feat_width))
    next_input = lax.all_to_all(copies, "dp", split_axis=0, concat_axis=0, tiled=True)
    return (layer_out, next_input)


def solution(mesh):
    in_specs = (
        P(None, "tp", "dp"),
        P("dp", None),
        P(("dp", "tp"), None),
        P(),
        P(),
        P(("dp", "tp"), None),
        P("tp", None, None),
        P("tp", None, None),
        P(),
    )
    out_specs = (P(("dp", "tp"), None), P(None, "tp", None))
    return jax.shard_map(local, mesh=mesh, in_specs=in_specs, out_specs=out_specs, check_vma=False)
```

```python
import jax
import jax.numpy as jnp
from jax import lax
from jax.sharding import PartitionSpec as P

EPS = 1e-05


def rms_scale(values, gain_vector):
    mean_square = jnp.mean(values * values, axis=-1, keepdims=True)
    return values * lax.rsqrt(mean_square + EPS) * gain_vector


def split_hi_lo(values):
    high = values.astype(jnp.bfloat16)
    low = (values - high.astype(jnp.float32)).astype(jnp.bfloat16)
    return high, low


def dp_reduce(blocks):
    ring = blocks.shape[0]
    here = lax.axis_index("dp")
    total = blocks[here]
    for shift in range(1, ring):
        sent = lax.dynamic_index_in_dim(blocks, (here + shift) % ring, axis=0, keepdims=False)
        pairs = [(j, (j + shift) % ring) for j in range(ring)]
        total = total + lax.ppermute(sent, "dp", pairs)
    return total


def local(attn_heads, w_out, residual, moe_gain, router, expert_ids, w_gate_up, w_down, next_gain):
    groups, tok_rows, quarter = attn_heads.shape
    feat_width = w_out.shape[1]
    experts = router.shape[1]
    top_count = expert_ids.shape[1]
    capacity = min(tok_rows, 3 * tok_rows * top_count // (2 * experts))
    slots = experts * capacity

    expert_pos = jnp.arange(experts, dtype=jnp.int32)
    chosen = expert_ids[:, :, None] == expert_pos[None, None, :]
    member = jnp.sum(chosen.astype(jnp.float32), axis=1)
    row_pos = jnp.arange(tok_rows, dtype=jnp.int32)
    earlier = (row_pos[None, :] < row_pos[:, None]).astype(jnp.bfloat16)
    row_ranks = jnp.dot(
        earlier, member.astype(jnp.bfloat16), preferred_element_type=jnp.float32
    ).astype(jnp.int32)
    slot_pos = jnp.arange(capacity, dtype=jnp.int32)
    placed = (member.T[:, None, :] > 0) & (row_ranks.T[:, None, :] == slot_pos[None, :, None])
    dispatch = placed.reshape(slots, tok_rows).astype(jnp.bfloat16)

    first = feat_width // 4
    bounds = [(0, first), (first, feat_width)]
    flat_heads = attn_heads.reshape(groups * tok_rows, quarter)
    partials = [
        jnp.dot(flat_heads, w_out[:, lo:hi], preferred_element_type=jnp.float32) for lo, hi in bounds
    ]
    pieces = lax.all_to_all(
        partials[0].reshape(groups, tok_rows, first), "dp", split_axis=0, concat_axis=0, tiled=True
    )
    part = jnp.sum(pieces, axis=0)
    mid_parts = []
    arrived_parts = []
    for c, (lo, hi) in enumerate(bounds):
        res_c, part = lax.optimization_barrier((residual[:, lo:hi], part))
        mid_c = (res_c.astype(jnp.float32) + part).astype(jnp.bfloat16)
        mid_parts.append(mid_c)
        outgoing = jnp.dot(dispatch, mid_c, preferred_element_type=jnp.float32).astype(jnp.bfloat16)
        if c == 0:
            outgoing, following = lax.optimization_barrier((outgoing, partials[1]))
            part = dp_reduce(following.reshape(groups, tok_rows, feat_width - first))
        arrived_parts.append(
            lax.all_to_all(
                outgoing.reshape(experts, capacity, hi - lo), "tp", split_axis=0, concat_axis=0, tiled=True
            ).reshape(slots, hi - lo)
        )
    mid_wide = jnp.concatenate(mid_parts, axis=1).astype(jnp.float32)
    normed = rms_scale(mid_wide, moe_gain).astype(jnp.bfloat16)
    logits = jnp.dot(normed, router, preferred_element_type=jnp.float32)

    picked = jnp.sum(jnp.where(chosen, logits[:, None, :], 0.0), axis=2)
    raised = jnp.exp(picked)
    gate_weights = raised / jnp.sum(raised, axis=1, keepdims=True)
    weight_full = jnp.sum(jnp.where(chosen, gate_weights[:, :, None], 0.0), axis=1)
    combine = jnp.where(placed, weight_full.T[:, None, :], 0.0).reshape(slots, tok_rows)
    combine_hi, combine_lo = split_hi_lo(combine)

    arrived_mid = jnp.concatenate(arrived_parts, axis=1).astype(jnp.float32)
    arrived = rms_scale(arrived_mid, moe_gain).astype(jnp.bfloat16)

    gate_up = w_gate_up[0]
    down_proj = w_down[0]
    hidden_width = down_proj.shape[0]
    projected_up = jnp.dot(arrived, gate_up, preferred_element_type=jnp.float32)
    activated = (
        jax.nn.silu(projected_up[:, :hidden_width]) * projected_up[:, hidden_width:]
    ).astype(jnp.bfloat16)
    served = jnp.dot(activated, down_proj, preferred_element_type=jnp.float32).astype(jnp.bfloat16)

    returned = lax.all_to_all(
        served.reshape(experts, capacity, feat_width), "tp", split_axis=0, concat_axis=0, tiled=True
    ).reshape(slots, feat_width)
    dims = (((0,), (0,)), ((), ()))
    expert_sum = lax.dot_general(
        combine_hi, returned, dims, preferred_element_type=jnp.float32
    ) + lax.dot_general(combine_lo, returned, dims, preferred_element_type=jnp.float32)

    layer_sum = mid_wide + expert_sum
    layer_out = layer_sum.astype(jnp.bfloat16)
    next_local = rms_scale(layer_sum, next_gain).astype(jnp.bfloat16)
    copies = jnp.broadcast_to(next_local[None], (groups, tok_rows, feat_width))
    next_input = lax.all_to_all(copies, "dp", split_axis=0, concat_axis=0, tiled=True)
    return (layer_out, next_input)


def solution(mesh):
    in_specs = (
        P(None, "tp", "dp"),
        P("dp", None),
        P(("dp", "tp"), None),
        P(),
        P(),
        P(("dp", "tp"), None),
        P("tp", None, None),
        P("tp", None, None),
        P(),
    )
    out_specs = (P(("dp", "tp"), None), P(None, "tp", None))
    return jax.shard_map(local, mesh=mesh, in_specs=in_specs, out_specs=out_specs, check_vma=False)
```

```python
import jax
import jax.numpy as jnp
from jax import lax
from jax.sharding import PartitionSpec as P


EPS = 1e-05


def rms_scale(values, gain_vector):
    mean_square = jnp.mean(values * values, axis=-1, keepdims=True)
    return values * lax.rsqrt(mean_square + EPS) * gain_vector


def split_hi_lo(values):
    high = values.astype(jnp.bfloat16)
    low = (values - high.astype(jnp.float32)).astype(jnp.bfloat16)
    return high, low


def dp_reduce(heads, weights):
    ring = heads.shape[0]
    here = lax.axis_index("dp")

    def product(group):
        rows = lax.dynamic_index_in_dim(heads, group, axis=0, keepdims=False)
        return jnp.dot(rows, weights, preferred_element_type=jnp.float32)

    total = product(here)
    for shift in range(1, ring):
        pairs = [(j, (j + shift) % ring) for j in range(ring)]
        total = total + lax.ppermute(product((here + shift) % ring), "dp", pairs)
    return total


def dp_gather(block):
    ring = lax.axis_size("dp")
    here = lax.axis_index("dp")
    received = [block]
    for shift in range(1, ring):
        pairs = [(j, (j + shift) % ring) for j in range(ring)]
        received.append(lax.ppermute(block, "dp", pairs))
    order = (here - jnp.arange(ring, dtype=jnp.int32)) % ring
    return jnp.take(jnp.stack(received), order, axis=0)


def local(attn_heads, w_out, residual, moe_gain, router, expert_ids, w_gate_up, w_down, next_gain):
    groups, tok_rows, quarter = attn_heads.shape
    feat_width = w_out.shape[1]
    experts = router.shape[1]
    top_count = expert_ids.shape[1]
    capacity = min(tok_rows, 3 * tok_rows * top_count // (2 * experts))
    slots = experts * capacity

    expert_pos = jnp.arange(experts, dtype=jnp.int32)
    chosen = expert_ids[:, :, None] == expert_pos[None, None, :]
    member = jnp.sum(chosen.astype(jnp.float32), axis=1)
    row_pos = jnp.arange(tok_rows, dtype=jnp.int32)
    earlier = (row_pos[None, :] < row_pos[:, None]).astype(jnp.bfloat16)
    row_ranks = jnp.dot(
        earlier, member.astype(jnp.bfloat16), preferred_element_type=jnp.float32
    ).astype(jnp.int32)
    slot_pos = jnp.arange(capacity, dtype=jnp.int32)
    placed = (member.T[:, None, :] > 0) & (row_ranks.T[:, None, :] == slot_pos[None, :, None])
    dispatch = placed.reshape(slots, tok_rows).astype(jnp.bfloat16)

    first = feat_width // 4
    bounds = [(0, first), (first, feat_width)]
    flat_heads = attn_heads.reshape(groups * tok_rows, quarter)
    partial = jnp.dot(flat_heads, w_out[:, :first], preferred_element_type=jnp.float32)
    pieces = lax.all_to_all(
        partial.reshape(groups, tok_rows, first), "dp", split_axis=0, concat_axis=0, tiled=True
    )
    part = jnp.sum(pieces, axis=0)
    mid_parts = []
    arrived_parts = []
    for c, (lo, hi) in enumerate(bounds):
        res_c, part = lax.optimization_barrier((residual[:, lo:hi], part))
        mid_c = (res_c.astype(jnp.float32) + part).astype(jnp.bfloat16)
        mid_parts.append(mid_c)
        outgoing = jnp.dot(dispatch, mid_c, preferred_element_type=jnp.float32).astype(jnp.bfloat16)
        if c == 0:
            outgoing, heads_now = lax.optimization_barrier((outgoing, attn_heads))
            part = dp_reduce(heads_now, w_out[:, first:])
        arrived_parts.append(
            lax.all_to_all(
                outgoing.reshape(experts, capacity, hi - lo), "tp", split_axis=0, concat_axis=0, tiled=True
            ).reshape(slots, hi - lo)
        )
    mid_wide = jnp.concatenate(mid_parts, axis=1).astype(jnp.float32)
    normed = rms_scale(mid_wide, moe_gain).astype(jnp.bfloat16)
    logits = jnp.dot(normed, router, preferred_element_type=jnp.float32)

    picked = jnp.sum(jnp.where(chosen, logits[:, None, :], 0.0), axis=2)
    raised = jnp.exp(picked)
    gate_weights = raised / jnp.sum(raised, axis=1, keepdims=True)
    weight_full = jnp.sum(jnp.where(chosen, gate_weights[:, :, None], 0.0), axis=1)
    combine = jnp.where(placed, weight_full.T[:, None, :], 0.0).reshape(slots, tok_rows)
    combine_hi, combine_lo = split_hi_lo(combine)

    arrived_mid = jnp.concatenate(arrived_parts, axis=1).astype(jnp.float32)
    arrived = rms_scale(arrived_mid, moe_gain).astype(jnp.bfloat16)

    gate_up = w_gate_up[0]
    down_proj = w_down[0]
    hidden_width = down_proj.shape[0]
    projected_up = jnp.dot(arrived, gate_up, preferred_element_type=jnp.float32)
    activated = (
        jax.nn.silu(projected_up[:, :hidden_width]) * projected_up[:, hidden_width:]
    ).astype(jnp.bfloat16)
    served = jnp.dot(activated, down_proj, preferred_element_type=jnp.float32).astype(jnp.bfloat16)

    served, combine_hi, combine_lo = lax.optimization_barrier((served, combine_hi, combine_lo))
    returned = lax.all_to_all(
        served.reshape(experts, capacity, feat_width), "tp", split_axis=0, concat_axis=0, tiled=True
    ).reshape(slots, feat_width)
    dims = (((0,), (0,)), ((), ()))
    expert_sum = lax.dot_general(
        combine_hi, returned, dims, preferred_element_type=jnp.float32
    ) + lax.dot_general(combine_lo, returned, dims, preferred_element_type=jnp.float32)

    layer_sum = mid_wide + expert_sum
    layer_out = layer_sum.astype(jnp.bfloat16)
    next_local = rms_scale(layer_sum, next_gain).astype(jnp.bfloat16)
    next_input = dp_gather(next_local)
    return (layer_out, next_input)


def solution(mesh):
    in_specs = (
        P(None, "tp", "dp"),
        P("dp", None),
        P(("dp", "tp"), None),
        P(),
        P(),
        P(("dp", "tp"), None),
        P("tp", None, None),
        P("tp", None, None),
        P(),
    )
    out_specs = (P(("dp", "tp"), None), P(None, "tp", None))

    return jax.shard_map(local, mesh=mesh, in_specs=in_specs, out_specs=out_specs, check_vma=False)
```

```python
import jax
import jax.numpy as jnp
from jax import lax
from jax.sharding import PartitionSpec as P


EPS = 1e-05


def rms_scale(values, gain_vector):
    mean_square = jnp.mean(values * values, axis=-1, keepdims=True)
    return values * lax.rsqrt(mean_square + EPS) * gain_vector


def split_hi_lo(values):
    high = values.astype(jnp.bfloat16)
    low = (values - high.astype(jnp.float32)).astype(jnp.bfloat16)
    return high, low


def dp_reduce(heads, weights):
    ring = heads.shape[0]
    here = lax.axis_index("dp")

    def product(group):
        rows = lax.dynamic_index_in_dim(heads, group, axis=0, keepdims=False)
        return jnp.dot(rows, weights, preferred_element_type=jnp.float32)

    total = product(here)
    for shift in range(1, ring):
        pairs = [(j, (j + shift) % ring) for j in range(ring)]
        total = total + lax.ppermute(product((here + shift) % ring), "dp", pairs)
    return total


def dp_gather(block):
    ring = lax.axis_size("dp")
    here = lax.axis_index("dp")
    gathered = jnp.zeros((ring,) + block.shape, block.dtype)
    for shift in range(ring):
        pairs = [(j, (j + shift) % ring) for j in range(ring)]
        piece = block if shift == 0 else lax.ppermute(block, "dp", pairs)
        gathered = lax.dynamic_update_index_in_dim(gathered, piece, (here - shift) % ring, axis=0)
    return gathered


def local(attn_heads, w_out, residual, moe_gain, router, expert_ids, w_gate_up, w_down, next_gain):
    groups, tok_rows, quarter = attn_heads.shape
    feat_width = w_out.shape[1]
    experts = router.shape[1]
    top_count = expert_ids.shape[1]
    capacity = min(tok_rows, 3 * tok_rows * top_count // (2 * experts))
    slots = experts * capacity

    expert_pos = jnp.arange(experts, dtype=jnp.int32)
    chosen = expert_ids[:, :, None] == expert_pos[None, None, :]
    member = jnp.sum(chosen.astype(jnp.float32), axis=1)
    row_pos = jnp.arange(tok_rows, dtype=jnp.int32)
    earlier = (row_pos[None, :] < row_pos[:, None]).astype(jnp.bfloat16)
    row_ranks = jnp.dot(
        earlier, member.astype(jnp.bfloat16), preferred_element_type=jnp.float32
    ).astype(jnp.int32)
    slot_pos = jnp.arange(capacity, dtype=jnp.int32)
    placed = (member.T[:, None, :] > 0) & (row_ranks.T[:, None, :] == slot_pos[None, :, None])
    dispatch = placed.reshape(slots, tok_rows).astype(jnp.bfloat16)

    first = feat_width // 4
    bounds = [(0, first), (first, feat_width)]
    flat_heads = attn_heads.reshape(groups * tok_rows, quarter)
    partial = jnp.dot(flat_heads, w_out[:, :first], preferred_element_type=jnp.float32)
    pieces = lax.all_to_all(
        partial.reshape(groups, tok_rows, first), "dp", split_axis=0, concat_axis=0, tiled=True
    )
    part = jnp.sum(pieces, axis=0)
    mid_parts = []
    arrived_parts = []
    for c, (lo, hi) in enumerate(bounds):
        res_c, part = lax.optimization_barrier((residual[:, lo:hi], part))
        mid_c = (res_c.astype(jnp.float32) + part).astype(jnp.bfloat16)
        mid_parts.append(mid_c)
        outgoing = jnp.dot(dispatch, mid_c, preferred_element_type=jnp.float32).astype(jnp.bfloat16)
        if c == 0:
            outgoing, heads_now = lax.optimization_barrier((outgoing, attn_heads))
            part = dp_reduce(heads_now, w_out[:, first:])
        arrived_parts.append(
            lax.all_to_all(
                outgoing.reshape(experts, capacity, hi - lo), "tp", split_axis=0, concat_axis=0, tiled=True
            ).reshape(slots, hi - lo)
        )
    mid_wide = jnp.concatenate(mid_parts, axis=1).astype(jnp.float32)
    normed = rms_scale(mid_wide, moe_gain).astype(jnp.bfloat16)
    logits = jnp.dot(normed, router, preferred_element_type=jnp.float32)

    picked = jnp.sum(jnp.where(chosen, logits[:, None, :], 0.0), axis=2)
    raised = jnp.exp(picked)
    gate_weights = raised / jnp.sum(raised, axis=1, keepdims=True)
    weight_full = jnp.sum(jnp.where(chosen, gate_weights[:, :, None], 0.0), axis=1)
    combine = jnp.where(placed, weight_full.T[:, None, :], 0.0).reshape(slots, tok_rows)
    combine_hi, combine_lo = split_hi_lo(combine)

    arrived_mid = jnp.concatenate(arrived_parts, axis=1).astype(jnp.float32)
    arrived = rms_scale(arrived_mid, moe_gain).astype(jnp.bfloat16)

    gate_up = w_gate_up[0]
    down_proj = w_down[0]
    hidden_width = down_proj.shape[0]
    projected_up = jnp.dot(arrived, gate_up, preferred_element_type=jnp.float32)
    activated = (
        jax.nn.silu(projected_up[:, :hidden_width]) * projected_up[:, hidden_width:]
    ).astype(jnp.bfloat16)
    served = jnp.dot(activated, down_proj, preferred_element_type=jnp.float32).astype(jnp.bfloat16)

    served, combine_hi, combine_lo = lax.optimization_barrier((served, combine_hi, combine_lo))
    returned = lax.all_to_all(
        served.reshape(experts, capacity, feat_width), "tp", split_axis=0, concat_axis=0, tiled=True
    ).reshape(slots, feat_width)
    dims = (((0,), (0,)), ((), ()))
    expert_sum = lax.dot_general(
        combine_hi, returned, dims, preferred_element_type=jnp.float32
    ) + lax.dot_general(combine_lo, returned, dims, preferred_element_type=jnp.float32)

    layer_sum = mid_wide + expert_sum
    layer_out = layer_sum.astype(jnp.bfloat16)
    next_local = rms_scale(layer_sum, next_gain).astype(jnp.bfloat16)
    next_input = dp_gather(next_local)
    return (layer_out, next_input)


def solution(mesh):
    in_specs = (
        P(None, "tp", "dp"),
        P("dp", None),
        P(("dp", "tp"), None),
        P(),
        P(),
        P(("dp", "tp"), None),
        P("tp", None, None),
        P("tp", None, None),
        P(),
    )
    out_specs = (P(("dp", "tp"), None), P(None, "tp", None))

    return jax.shard_map(local, mesh=mesh, in_specs=in_specs, out_specs=out_specs, check_vma=False)
```

```python
import jax
import jax.numpy as jnp
from jax import lax
from jax.sharding import PartitionSpec as P


EPS = 1e-05


def rms_scale(values, gain_vector):
    mean_square = jnp.mean(values * values, axis=-1, keepdims=True)
    return values * lax.rsqrt(mean_square + EPS) * gain_vector


def split_hi_lo(values):
    high = values.astype(jnp.bfloat16)
    low = (values - high.astype(jnp.float32)).astype(jnp.bfloat16)
    return high, low


def dp_reduce(heads, weights):
    ring = heads.shape[0]
    here = lax.axis_index("dp")

    def product(group):
        rows = lax.dynamic_index_in_dim(heads, group, axis=0, keepdims=False)
        return jnp.dot(rows, weights, preferred_element_type=jnp.float32)

    total = product(here)
    for shift in range(1, ring):
        pairs = [(j, (j + shift) % ring) for j in range(ring)]
        total = total + lax.ppermute(product((here + shift) % ring), "dp", pairs)
    return total


def local(attn_heads, w_out, residual, moe_gain, router, expert_ids, w_gate_up, w_down, next_gain):
    groups, tok_rows, quarter = attn_heads.shape
    feat_width = w_out.shape[1]
    experts = router.shape[1]
    top_count = expert_ids.shape[1]
    capacity = min(tok_rows, 3 * tok_rows * top_count // (2 * experts))
    slots = experts * capacity

    expert_pos = jnp.arange(experts, dtype=jnp.int32)
    chosen = expert_ids[:, :, None] == expert_pos[None, None, :]
    member = jnp.sum(chosen.astype(jnp.float32), axis=1)
    row_pos = jnp.arange(tok_rows, dtype=jnp.int32)
    earlier = (row_pos[None, :] < row_pos[:, None]).astype(jnp.bfloat16)
    row_ranks = jnp.dot(
        earlier, member.astype(jnp.bfloat16), preferred_element_type=jnp.float32
    ).astype(jnp.int32)
    slot_pos = jnp.arange(capacity, dtype=jnp.int32)
    placed = (member.T[:, None, :] > 0) & (row_ranks.T[:, None, :] == slot_pos[None, :, None])
    dispatch = placed.reshape(slots, tok_rows).astype(jnp.bfloat16)

    first = feat_width // 4
    bounds = [(0, first), (first, 2 * first), (2 * first, feat_width)]
    flat_heads = attn_heads.reshape(groups * tok_rows, quarter)
    partial = jnp.dot(flat_heads, w_out[:, :first], preferred_element_type=jnp.float32)
    pieces = lax.all_to_all(
        partial.reshape(groups, tok_rows, first), "dp", split_axis=0, concat_axis=0, tiled=True
    )
    part = jnp.sum(pieces, axis=0)
    mid_parts = []
    arrived_parts = []
    for c, (lo, hi) in enumerate(bounds):
        res_c, part = lax.optimization_barrier((residual[:, lo:hi], part))
        mid_c = (res_c.astype(jnp.float32) + part).astype(jnp.bfloat16)
        mid_parts.append(mid_c)
        outgoing = jnp.dot(dispatch, mid_c, preferred_element_type=jnp.float32).astype(jnp.bfloat16)
        if c + 1 < len(bounds):
            outgoing, heads_now = lax.optimization_barrier((outgoing, attn_heads))
            next_lo, next_hi = bounds[c + 1]
            part = dp_reduce(heads_now, w_out[:, next_lo:next_hi])
        arrived_parts.append(
            lax.all_to_all(
                outgoing.reshape(experts, capacity, hi - lo), "tp", split_axis=0, concat_axis=0, tiled=True
            ).reshape(slots, hi - lo)
        )
    mid_wide = jnp.concatenate(mid_parts, axis=1).astype(jnp.float32)
    normed = rms_scale(mid_wide, moe_gain).astype(jnp.bfloat16)
    logits = jnp.dot(normed, router, preferred_element_type=jnp.float32)

    picked = jnp.sum(jnp.where(chosen, logits[:, None, :], 0.0), axis=2)
    raised = jnp.exp(picked)
    gate_weights = raised / jnp.sum(raised, axis=1, keepdims=True)
    weight_full = jnp.sum(jnp.where(chosen, gate_weights[:, :, None], 0.0), axis=1)
    combine = jnp.where(placed, weight_full.T[:, None, :], 0.0).reshape(slots, tok_rows)
    combine_hi, combine_lo = split_hi_lo(combine)

    arrived_mid = jnp.concatenate(arrived_parts, axis=1).astype(jnp.float32)
    arrived = rms_scale(arrived_mid, moe_gain).astype(jnp.bfloat16)

    gate_up = w_gate_up[0]
    down_proj = w_down[0]
    hidden_width = down_proj.shape[0]
    projected_up = jnp.dot(arrived, gate_up, preferred_element_type=jnp.float32)
    activated = (
        jax.nn.silu(projected_up[:, :hidden_width]) * projected_up[:, hidden_width:]
    ).astype(jnp.bfloat16)
    served = jnp.dot(activated, down_proj, preferred_element_type=jnp.float32).astype(jnp.bfloat16)

    served, combine_hi, combine_lo = lax.optimization_barrier((served, combine_hi, combine_lo))
    returned = lax.all_to_all(
        served.reshape(experts, capacity, feat_width), "tp", split_axis=0, concat_axis=0, tiled=True
    ).reshape(slots, feat_width)
    dims = (((0,), (0,)), ((), ()))
    expert_sum = lax.dot_general(
        combine_hi, returned, dims, preferred_element_type=jnp.float32
    ) + lax.dot_general(combine_lo, returned, dims, preferred_element_type=jnp.float32)

    layer_sum = mid_wide + expert_sum
    layer_out = layer_sum.astype(jnp.bfloat16)
    next_local = rms_scale(layer_sum, next_gain).astype(jnp.bfloat16)
    copies = jnp.broadcast_to(next_local[None], (groups, tok_rows, feat_width))
    next_input = lax.all_to_all(copies, "dp", split_axis=0, concat_axis=0, tiled=True)
    return (layer_out, next_input)


def solution(mesh):
    in_specs = (
        P(None, "tp", "dp"),
        P("dp", None),
        P(("dp", "tp"), None),
        P(),
        P(),
        P(("dp", "tp"), None),
        P("tp", None, None),
        P("tp", None, None),
        P(),
    )
    out_specs = (P(("dp", "tp"), None), P(None, "tp", None))

    return jax.shard_map(local, mesh=mesh, in_specs=in_specs, out_specs=out_specs, check_vma=False)
```

```python
import jax
import jax.numpy as jnp
from jax import lax
from jax.sharding import PartitionSpec as P


EPS = 1e-05


def rms_scale(values, gain_vector):
    mean_square = jnp.mean(values * values, axis=-1, keepdims=True)
    return values * lax.rsqrt(mean_square + EPS) * gain_vector


def split_hi_lo(values):
    high = values.astype(jnp.bfloat16)
    low = (values - high.astype(jnp.float32)).astype(jnp.bfloat16)
    return high, low


def dp_reduce(heads, weights):
    ring = heads.shape[0]
    here = lax.axis_index("dp")

    def product(group):
        rows = lax.dynamic_index_in_dim(heads, group, axis=0, keepdims=False)
        return jnp.dot(rows, weights, preferred_element_type=jnp.float32)

    total = product(here)
    for shift in range(1, ring):
        pairs = [(j, (j + shift) % ring) for j in range(ring)]
        total = total + lax.ppermute(product((here + shift) % ring), "dp", pairs)
    return total


def local(attn_heads, w_out, residual, moe_gain, router, expert_ids, w_gate_up, w_down, next_gain):
    groups, tok_rows, quarter = attn_heads.shape
    feat_width = w_out.shape[1]
    experts = router.shape[1]
    top_count = expert_ids.shape[1]
    capacity = min(tok_rows, 3 * tok_rows * top_count // (2 * experts))
    slots = experts * capacity

    expert_pos = jnp.arange(experts, dtype=jnp.int32)
    chosen = expert_ids[:, :, None] == expert_pos[None, None, :]
    member = jnp.sum(chosen.astype(jnp.float32), axis=1)
    row_pos = jnp.arange(tok_rows, dtype=jnp.int32)
    earlier = (row_pos[None, :] < row_pos[:, None]).astype(jnp.bfloat16)
    row_ranks = jnp.dot(
        earlier, member.astype(jnp.bfloat16), preferred_element_type=jnp.float32
    ).astype(jnp.int32)
    slot_pos = jnp.arange(capacity, dtype=jnp.int32)
    placed = (member.T[:, None, :] > 0) & (row_ranks.T[:, None, :] == slot_pos[None, :, None])
    dispatch = placed.reshape(slots, tok_rows).astype(jnp.bfloat16)

    first = feat_width // 4
    bounds = [(0, first), (first, feat_width)]
    flat_heads = attn_heads.reshape(groups * tok_rows, quarter)
    partial = jnp.dot(flat_heads, w_out[:, :first], preferred_element_type=jnp.float32)
    pieces = lax.all_to_all(
        partial.reshape(groups, tok_rows, first), "dp", split_axis=0, concat_axis=0, tiled=True
    )
    part = jnp.sum(pieces, axis=0)
    mid_parts = []
    arrived_parts = []
    for c, (lo, hi) in enumerate(bounds):
        res_c, part = lax.optimization_barrier((residual[:, lo:hi], part))
        mid_c = (res_c.astype(jnp.float32) + part).astype(jnp.bfloat16)
        mid_parts.append(mid_c)
        outgoing = jnp.dot(dispatch, mid_c, preferred_element_type=jnp.float32).astype(jnp.bfloat16)
        if c == 0:
            outgoing, heads_now = lax.optimization_barrier((outgoing, attn_heads))
            part = dp_reduce(heads_now, w_out[:, first:])
        arrived_parts.append(
            lax.all_to_all(
                outgoing.reshape(experts, capacity, hi - lo), "tp", split_axis=0, concat_axis=0, tiled=True
            ).reshape(slots, hi - lo)
        )
    mid_wide = jnp.concatenate(mid_parts, axis=1).astype(jnp.float32)
    normed = rms_scale(mid_wide, moe_gain).astype(jnp.bfloat16)
    logits = jnp.dot(normed, router, preferred_element_type=jnp.float32)

    picked = jnp.sum(jnp.where(chosen, logits[:, None, :], 0.0), axis=2)
    raised = jnp.exp(picked)
    gate_weights = raised / jnp.sum(raised, axis=1, keepdims=True)
    weight_full = jnp.sum(jnp.where(chosen, gate_weights[:, :, None], 0.0), axis=1)
    combine = jnp.where(placed, weight_full.T[:, None, :], 0.0).reshape(slots, tok_rows)
    combine_hi, combine_lo = split_hi_lo(combine)

    gate_up = w_gate_up[0]
    down_proj = w_down[0]
    hidden_width = down_proj.shape[0]
    arrived_wide = [p.astype(jnp.float32) for p in arrived_parts]
    square_sum = sum(jnp.sum(p * p, axis=-1, keepdims=True) for p in arrived_wide)
    scale = lax.rsqrt(square_sum / feat_width + EPS)
    projected_up = sum(
        jnp.dot(
            (p * scale * moe_gain[lo:hi]).astype(jnp.bfloat16),
            gate_up[lo:hi],
            preferred_element_type=jnp.float32,
        )
        for p, (lo, hi) in zip(arrived_wide, bounds)
    )
    activated = (
        jax.nn.silu(projected_up[:, :hidden_width]) * projected_up[:, hidden_width:]
    ).astype(jnp.bfloat16)
    served = jnp.dot(activated, down_proj, preferred_element_type=jnp.float32).astype(jnp.bfloat16)

    served, combine_hi, combine_lo = lax.optimization_barrier((served, combine_hi, combine_lo))
    returned = lax.all_to_all(
        served.reshape(experts, capacity, feat_width), "tp", split_axis=0, concat_axis=0, tiled=True
    ).reshape(slots, feat_width)
    dims = (((0,), (0,)), ((), ()))
    expert_sum = lax.dot_general(
        combine_hi, returned, dims, preferred_element_type=jnp.float32
    ) + lax.dot_general(combine_lo, returned, dims, preferred_element_type=jnp.float32)

    layer_sum = mid_wide + expert_sum
    layer_out = layer_sum.astype(jnp.bfloat16)
    next_local = rms_scale(layer_sum, next_gain).astype(jnp.bfloat16)
    copies = jnp.broadcast_to(next_local[None], (groups, tok_rows, feat_width))
    next_input = lax.all_to_all(copies, "dp", split_axis=0, concat_axis=0, tiled=True)
    return (layer_out, next_input)


def solution(mesh):
    in_specs = (
        P(None, "tp", "dp"),
        P("dp", None),
        P(("dp", "tp"), None),
        P(),
        P(),
        P(("dp", "tp"), None),
        P("tp", None, None),
        P("tp", None, None),
        P(),
    )
    out_specs = (P(("dp", "tp"), None), P(None, "tp", None))

    return jax.shard_map(local, mesh=mesh, in_specs=in_specs, out_specs=out_specs, check_vma=False)
```

```python
import jax
import jax.numpy as jnp
from jax import lax
from jax.sharding import PartitionSpec as P


EPS = 1e-05


def rms_scale(values, gain_vector):
    mean_square = jnp.mean(values * values, axis=-1, keepdims=True)
    return values * lax.rsqrt(mean_square + EPS) * gain_vector


def split_hi_lo(values):
    high = values.astype(jnp.bfloat16)
    low = (values - high.astype(jnp.float32)).astype(jnp.bfloat16)
    return high, low


def dp_reduce(heads, weights):
    ring = heads.shape[0]
    here = lax.axis_index("dp")

    def product(group):
        rows = lax.dynamic_index_in_dim(heads, group, axis=0, keepdims=False)
        return jnp.dot(rows, weights, preferred_element_type=jnp.float32)

    total = product(here)
    for shift in range(1, ring):
        pairs = [(j, (j + shift) % ring) for j in range(ring)]
        total = total + lax.ppermute(product((here + shift) % ring), "dp", pairs)
    return total


def local(attn_heads, w_out, residual, moe_gain, router, expert_ids, w_gate_up, w_down, next_gain):
    groups, tok_rows, quarter = attn_heads.shape
    feat_width = w_out.shape[1]
    experts = router.shape[1]
    top_count = expert_ids.shape[1]
    capacity = min(tok_rows, 3 * tok_rows * top_count // (2 * experts))
    slots = experts * capacity

    expert_pos = jnp.arange(experts, dtype=jnp.int32)
    chosen = expert_ids[:, :, None] == expert_pos[None, None, :]
    member = jnp.sum(chosen.astype(jnp.float32), axis=1)
    row_pos = jnp.arange(tok_rows, dtype=jnp.int32)
    earlier = (row_pos[None, :] < row_pos[:, None]).astype(jnp.bfloat16)
    row_ranks = jnp.dot(
        earlier, member.astype(jnp.bfloat16), preferred_element_type=jnp.float32
    ).astype(jnp.int32)
    slot_pos = jnp.arange(capacity, dtype=jnp.int32)
    placed = (member.T[:, None, :] > 0) & (row_ranks.T[:, None, :] == slot_pos[None, :, None])
    dispatch = placed.reshape(slots, tok_rows).astype(jnp.bfloat16)

    first = 5 * feat_width // 16
    bounds = [(0, first), (first, feat_width)]
    flat_heads = attn_heads.reshape(groups * tok_rows, quarter)
    partial = jnp.dot(flat_heads, w_out[:, :first], preferred_element_type=jnp.float32)
    pieces = lax.all_to_all(
        partial.reshape(groups, tok_rows, first), "dp", split_axis=0, concat_axis=0, tiled=True
    )
    part = jnp.sum(pieces, axis=0)
    mid_parts = []
    arrived_parts = []
    for c, (lo, hi) in enumerate(bounds):
        res_c, part = lax.optimization_barrier((residual[:, lo:hi], part))
        mid_c = (res_c.astype(jnp.float32) + part).astype(jnp.bfloat16)
        mid_parts.append(mid_c)
        outgoing = jnp.dot(dispatch, mid_c, preferred_element_type=jnp.float32).astype(jnp.bfloat16)
        if c == 0:
            outgoing, heads_now = lax.optimization_barrier((outgoing, attn_heads))
            part = dp_reduce(heads_now, w_out[:, first:])
        arrived_parts.append(
            lax.all_to_all(
                outgoing.reshape(experts, capacity, hi - lo), "tp", split_axis=0, concat_axis=0, tiled=True
            ).reshape(slots, hi - lo)
        )
    mid_wide = jnp.concatenate(mid_parts, axis=1).astype(jnp.float32)
    normed = rms_scale(mid_wide, moe_gain).astype(jnp.bfloat16)
    logits = jnp.dot(normed, router, preferred_element_type=jnp.float32)

    picked = jnp.sum(jnp.where(chosen, logits[:, None, :], 0.0), axis=2)
    raised = jnp.exp(picked)
    gate_weights = raised / jnp.sum(raised, axis=1, keepdims=True)
    weight_full = jnp.sum(jnp.where(chosen, gate_weights[:, :, None], 0.0), axis=1)
    combine = jnp.where(placed, weight_full.T[:, None, :], 0.0).reshape(slots, tok_rows)
    combine_hi, combine_lo = split_hi_lo(combine)

    arrived_mid = jnp.concatenate(arrived_parts, axis=1).astype(jnp.float32)
    arrived = rms_scale(arrived_mid, moe_gain).astype(jnp.bfloat16)

    gate_up = w_gate_up[0]
    down_proj = w_down[0]
    hidden_width = down_proj.shape[0]
    projected_up = jnp.dot(arrived, gate_up, preferred_element_type=jnp.float32)
    activated = (
        jax.nn.silu(projected_up[:, :hidden_width]) * projected_up[:, hidden_width:]
    ).astype(jnp.bfloat16)
    served = jnp.dot(activated, down_proj, preferred_element_type=jnp.float32).astype(jnp.bfloat16)

    served, combine_hi, combine_lo = lax.optimization_barrier((served, combine_hi, combine_lo))
    returned = lax.all_to_all(
        served.reshape(experts, capacity, feat_width), "tp", split_axis=0, concat_axis=0, tiled=True
    ).reshape(slots, feat_width)
    dims = (((0,), (0,)), ((), ()))
    expert_sum = lax.dot_general(
        combine_hi, returned, dims, preferred_element_type=jnp.float32
    ) + lax.dot_general(combine_lo, returned, dims, preferred_element_type=jnp.float32)

    layer_sum = mid_wide + expert_sum
    layer_out = layer_sum.astype(jnp.bfloat16)
    next_local = rms_scale(layer_sum, next_gain).astype(jnp.bfloat16)
    copies = jnp.broadcast_to(next_local[None], (groups, tok_rows, feat_width))
    next_input = lax.all_to_all(copies, "dp", split_axis=0, concat_axis=0, tiled=True)
    return (layer_out, next_input)


def solution(mesh):
    in_specs = (
        P(None, "tp", "dp"),
        P("dp", None),
        P(("dp", "tp"), None),
        P(),
        P(),
        P(("dp", "tp"), None),
        P("tp", None, None),
        P("tp", None, None),
        P(),
    )
    out_specs = (P(("dp", "tp"), None), P(None, "tp", None))

    return jax.shard_map(local, mesh=mesh, in_specs=in_specs, out_specs=out_specs, check_vma=False)
```

```python
import jax
import jax.numpy as jnp
from jax import lax
from jax.sharding import PartitionSpec as P


EPS = 1e-05


def rms_scale(values, gain_vector):
    mean_square = jnp.mean(values * values, axis=-1, keepdims=True)
    return values * lax.rsqrt(mean_square + EPS) * gain_vector


def split_hi_lo(values):
    high = values.astype(jnp.bfloat16)
    low = (values - high.astype(jnp.float32)).astype(jnp.bfloat16)
    return high, low


def dp_reduce(heads, weights):
    ring = heads.shape[0]
    here = lax.axis_index("dp")

    def product(group):
        rows = lax.dynamic_index_in_dim(heads, group, axis=0, keepdims=False)
        return jnp.dot(rows, weights, preferred_element_type=jnp.float32)

    total = product(here)
    for shift in range(1, ring):
        pairs = [(j, (j + shift) % ring) for j in range(ring)]
        total = total + lax.ppermute(product((here + shift) % ring), "dp", pairs)
    return total


def local(attn_heads, w_out, residual, moe_gain, router, expert_ids, w_gate_up, w_down, next_gain):
    groups, tok_rows, _ = attn_heads.shape
    feat_width = w_out.shape[1]
    experts = router.shape[1]
    top_count = expert_ids.shape[1]
    capacity = min(tok_rows, 3 * tok_rows * top_count // (2 * experts))
    slots = experts * capacity

    expert_pos = jnp.arange(experts, dtype=jnp.int32)
    chosen = expert_ids[:, :, None] == expert_pos[None, None, :]
    member = jnp.sum(chosen.astype(jnp.float32), axis=1)
    row_pos = jnp.arange(tok_rows, dtype=jnp.int32)
    earlier = (row_pos[None, :] < row_pos[:, None]).astype(jnp.bfloat16)
    row_ranks = jnp.dot(
        earlier, member.astype(jnp.bfloat16), preferred_element_type=jnp.float32
    ).astype(jnp.int32)
    slot_pos = jnp.arange(capacity, dtype=jnp.int32)
    placed = (member.T[:, None, :] > 0) & (row_ranks.T[:, None, :] == slot_pos[None, :, None])
    dispatch = placed.reshape(slots, tok_rows).astype(jnp.bfloat16)

    first = feat_width // 4
    bounds = [(0, first), (first, feat_width)]
    part = dp_reduce(attn_heads, w_out[:, :first])
    mid_parts = []
    arrived_parts = []
    for c, (lo, hi) in enumerate(bounds):
        res_c, part = lax.optimization_barrier((residual[:, lo:hi], part))
        mid_c = (res_c.astype(jnp.float32) + part).astype(jnp.bfloat16)
        mid_parts.append(mid_c)
        outgoing = jnp.dot(dispatch, mid_c, preferred_element_type=jnp.float32).astype(jnp.bfloat16)
        if c == 0:
            outgoing, heads_now = lax.optimization_barrier((outgoing, attn_heads))
            part = dp_reduce(heads_now, w_out[:, first:])
        arrived_parts.append(
            lax.all_to_all(
                outgoing.reshape(experts, capacity, hi - lo), "tp", split_axis=0, concat_axis=0, tiled=True
            ).reshape(slots, hi - lo)
        )
    mid_wide = jnp.concatenate(mid_parts, axis=1).astype(jnp.float32)
    normed = rms_scale(mid_wide, moe_gain).astype(jnp.bfloat16)
    logits = jnp.dot(normed, router, preferred_element_type=jnp.float32)

    picked = jnp.sum(jnp.where(chosen, logits[:, None, :], 0.0), axis=2)
    raised = jnp.exp(picked)
    gate_weights = raised / jnp.sum(raised, axis=1, keepdims=True)
    weight_full = jnp.sum(jnp.where(chosen, gate_weights[:, :, None], 0.0), axis=1)
    combine = jnp.where(placed, weight_full.T[:, None, :], 0.0).reshape(slots, tok_rows)
    combine_hi, combine_lo = split_hi_lo(combine)

    arrived_mid = jnp.concatenate(arrived_parts, axis=1).astype(jnp.float32)
    arrived = rms_scale(arrived_mid, moe_gain).astype(jnp.bfloat16)

    gate_up = w_gate_up[0]
    down_proj = w_down[0]
    hidden_width = down_proj.shape[0]
    projected_up = jnp.dot(arrived, gate_up, preferred_element_type=jnp.float32)
    activated = (
        jax.nn.silu(projected_up[:, :hidden_width]) * projected_up[:, hidden_width:]
    ).astype(jnp.bfloat16)
    served = jnp.dot(activated, down_proj, preferred_element_type=jnp.float32).astype(jnp.bfloat16)

    served, combine_hi, combine_lo = lax.optimization_barrier((served, combine_hi, combine_lo))
    returned = lax.all_to_all(
        served.reshape(experts, capacity, feat_width), "tp", split_axis=0, concat_axis=0, tiled=True
    ).reshape(slots, feat_width)
    dims = (((0,), (0,)), ((), ()))
    expert_sum = lax.dot_general(
        combine_hi, returned, dims, preferred_element_type=jnp.float32
    ) + lax.dot_general(combine_lo, returned, dims, preferred_element_type=jnp.float32)

    layer_sum = mid_wide + expert_sum
    layer_out = layer_sum.astype(jnp.bfloat16)
    next_local = rms_scale(layer_sum, next_gain).astype(jnp.bfloat16)
    copies = jnp.broadcast_to(next_local[None], (groups, tok_rows, feat_width))
    next_input = lax.all_to_all(copies, "dp", split_axis=0, concat_axis=0, tiled=True)
    return (layer_out, next_input)


def solution(mesh):
    in_specs = (
        P(None, "tp", "dp"),
        P("dp", None),
        P(("dp", "tp"), None),
        P(),
        P(),
        P(("dp", "tp"), None),
        P("tp", None, None),
        P("tp", None, None),
        P(),
    )
    out_specs = (P(("dp", "tp"), None), P(None, "tp", None))

    return jax.shard_map(local, mesh=mesh, in_specs=in_specs, out_specs=out_specs, check_vma=False)
```
